256 devices in a mesh: blk: 64 (over y, x_lo, z), team: 4 (over x_hi, core).
Axes of the slice: x: 4 (x_hi: 2, x_lo: 2; x = x_hi * 2 + x_lo), y: 4, z: 8, core: 2. Of those that a mesh axis runs over, the one named last changes fastest.
Arguments:
- loadings: bfloat16 [64, 98304], P(None, ('blk', 'team')), may hold values from -6 to 6
- scales: bfloat16 [64, 768], P(None, ('blk', 'team')), may hold values from 0.25 to 4
- cov: bfloat16 [16384, 16, 4, 1536], P('blk', None, 'team'), may hold values from -0.01953125 to 0.01953125
Outputs:
- product: float32 [64, 16384], P(None, 'blk')
The draws below stay inside these ranges and needn't reach their ends.
All inputs are finite; a program needn't handle non-finite values.
Results may differ from the reference program's by a relative error of at most 0.0028.
Values may be sent and summed in bfloat16 or wider, within the bound.
No kernel may reach another device: no remote copies, remote signals or barrier semaphores. Data moves between devices by JAX's collectives and lax.ppermute only.
A program may use at most 128 MiB of HBM per device.

```python
import math
import jax
import jax.numpy as jnp
from jax import lax

M = 98304
K = 64
GROUP = 128
ROWS = 16384
STOPS = 16
BLOCK = 1536
N_TEAM = 4


def steps_of(key, dims, pieces, smallest, largest):
    loudness, own = 1.0, jax.random.fold_in(key, 6)
    for dim, blocks in pieces:
        heights = jnp.exp(jax.random.uniform(jax.random.fold_in(own, dim), (blocks,), jnp.float32, smallest / len(pieces), largest / len(pieces)))
        loudness = loudness * jnp.repeat(heights, dims[dim] // blocks).reshape([-1 if axis == dim else 1 for axis in range(len(dims))])
    return loudness


def normal_values(rng, dims, scale, bound, shards=(), held_as=jnp.bfloat16):
    factor_of = steps_of(rng, dims, shards, -0.22, 0.18) if shards else 1.0
    entries = jax.random.normal(rng, dims, jnp.float32) * scale * factor_of
    return jnp.minimum(jnp.maximum(entries, -bound), bound).astype(held_as)


def setup_inputs(seed: int = 0) -> dict:
    key_of = jax.random.split(jax.random.key(seed), 4)
    return {
        "loadings": normal_values(key_of[0], (K, M), 1.0, 6.0, ((1, 256),)),
        "scales": jnp.clip(jnp.exp(math.log(4.0) - 2.7725887 * jax.random.uniform(key_of[1], (K, M // GROUP), jnp.float32) ** steps_of(key_of[1], (K, M // GROUP), ((1, 256),), -0.2, 0.2)), 0.25, 4.0).astype(jnp.bfloat16),
        "cov": normal_values(key_of[2], (ROWS, STOPS, N_TEAM, BLOCK), M ** -0.5, 0.01953125, ((0, 64), (2, 4))),
    }


def reference(loadings, scales, cov):
    n_loads = loadings.shape[0]
    n_cols = loadings.shape[1]
    scaled = (loadings.astype(jnp.float32).reshape(n_loads, n_cols // GROUP, GROUP) * scales.astype(jnp.float32)[:, :, None]).reshape(n_loads, n_cols).astype(jnp.bfloat16)
    cov_rows = cov.reshape(ROWS, M)
    col_width = math.gcd(M, 8192)
    col_blocks = M // col_width

    def add_block(running, block_idx):
        start = (block_idx * col_width).astype(jnp.int32)
        columns = lax.dynamic_slice_in_dim(cov_rows, start, col_width, 1)
        part = lax.dynamic_slice_in_dim(scaled, start, col_width, 1)
        term = lax.dot_general(part, columns, (((1,), (1,)), ((), ())), preferred_element_type=jnp.float32)
        return running + term, None

    initial = jnp.zeros((n_loads, ROWS), jnp.float32)
    result, _ = lax.scan(add_block, initial, jnp.arange(col_blocks, dtype=jnp.int32))
    return result
```

```python
import jax
import jax.numpy as jnp
from jax import lax
from jax.sharding import PartitionSpec as P


def per_device(loadings, scales, cov):
    n_loads, width = loadings.shape
    groups = scales.shape[1]
    team_size = lax.axis_size("team")
    blk_size = lax.axis_size("blk")
    scaled = (
        loadings.astype(jnp.float32).reshape(n_loads, groups, width // groups)
        * scales.astype(jnp.float32)[:, :, None]
    ).reshape(n_loads, width).astype(jnp.bfloat16)
    pairs = []
    for b in range(blk_size):
        c, d = divmod(b, team_size)
        for p in range(team_size):
            pairs.append((b * team_size + p, (c * team_size + p) * team_size + d))
    moved = lax.ppermute(scaled, ("blk", "team"), pairs)
    gathered = lax.all_gather(moved, "blk", axis=1, tiled=True)
    stops = cov.shape[1]
    gathered = gathered.reshape(n_loads, stops, cov.shape[3])
    cov_local = cov[:, :, 0, :]
    part = lax.dot_general(
        gathered, cov_local, (((1, 2), (1, 2)), ((), ())), preferred_element_type=jnp.float32
    )
    return lax.psum(part, "team")


def solution(mesh):
    placed = (P(None, ("blk", "team")), P(None, ("blk", "team")), P("blk", None, "team", None))
    return jax.shard_map(
        per_device, mesh=mesh, in_specs=placed, out_specs=P(None, "blk"), check_vma=False
    )
```

```python
import jax
import jax.numpy as jnp
import numpy as np
from jax import lax
from jax.sharding import Mesh
from jax.sharding import PartitionSpec as P

SUB = (("y", 4), ("xl", 2), ("z", 8), ("xh", 2), ("core", 2))
BLK = ("y", "xl", "z")
TEAM = ("xh", "core")


def ring_gather(x, axis):
    n = lax.axis_size(axis)
    if n == 1:
        return x[None]
    fwd, bwd = x, x
    got = {0: x}
    for s in range(1, n // 2 + 1):
        fwd = lax.ppermute(fwd, axis, [(i, (i + 1) % n) for i in range(n)])
        got[-s] = fwd
        if s <= (n - 1) // 2:
            bwd = lax.ppermute(bwd, axis, [(i, (i - 1) % n) for i in range(n)])
            got[s] = bwd
    rel = [got[k] if k in got else got[k - n] for k in range(n)]
    rel = jnp.stack(rel + rel)
    me = lax.axis_index(axis)
    return lax.dynamic_slice_in_dim(rel, (n - me) % n, n, 0)


def team_sum(x):
    other = lax.ppermute(x, "core", [(0, 1), (1, 0)])
    x = x + other
    other = lax.ppermute(x, "xh", [(0, 1), (1, 0)])
    return x + other


def per_device(loadings, scales, cov):
    n_loads, width = loadings.shape
    groups = scales.shape[1]
    scaled = (
        loadings.astype(jnp.float32).reshape(n_loads, groups, width // groups)
        * scales.astype(jnp.float32)[:, :, None]
    ).reshape(n_loads, width).astype(jnp.bfloat16)
    nz = lax.axis_size("z")
    pairs = []
    for z in range(nz):
        for t in range(4):
            zh, d = divmod(z, 4)
            pairs.append((z * 4 + t, (zh * 4 + t) * 4 + d))
    moved = lax.ppermute(scaled, ("z", "xh", "core"), pairs)
    half = width // 2
    part_a, part_b = moved[:, :half], moved[:, half:]
    ga = ring_gather(ring_gather(ring_gather(part_a, "xl"), "y"), "z")
    gb = ring_gather(ring_gather(ring_gather(part_b, "xl"), "z"), "y")
    ga = jnp.transpose(ga, (1, 2, 0, 3, 4))
    gb = jnp.transpose(gb, (0, 2, 1, 3, 4))
    both = jnp.concatenate([ga, gb], axis=-1)
    ny, nx = both.shape[0], both.shape[1]
    stops = cov.shape[1]
    both = both.reshape(ny, nx, nz // 4, 4, n_loads, width)
    both = jnp.transpose(both, (4, 0, 1, 2, 3, 5)).reshape(n_loads, stops, cov.shape[3])
    cov_local = cov[:, :, 0, :]
    part = lax.dot_general(
        both, cov_local, (((1, 2), (1, 2)), ((), ())), preferred_element_type=jnp.float32
    )
    return team_sum(part)


def solution(mesh):
    sizes = tuple(s for _, s in SUB)
    assert mesh.devices.size == int(np.prod(sizes))
    fine = Mesh(mesh.devices.reshape(sizes), tuple(n for n, _ in SUB))
    placed = (P(None, BLK + TEAM), P(None, BLK + TEAM), P(BLK, None, TEAM, None))
    return jax.shard_map(
        per_device, mesh=fine, in_specs=placed, out_specs=P(None, BLK), check_vma=False
    )
```

```python
import jax
import jax.numpy as jnp
import numpy as np
from jax import lax
from jax.sharding import Mesh
from jax.sharding import PartitionSpec as P

SUB = (("y", 4), ("xl", 2), ("z", 8), ("xh", 2), ("core", 2))
BLK = ("y", "xl", "z")
TEAM = ("xh", "core")


def shifted(x, axis, by):
    n = lax.axis_size(axis)
    return lax.ppermute(x, axis, [(i, (i + by) % n) for i in range(n)])


def ring_gather(x, axis):
    n = lax.axis_size(axis)
    fwd, bwd = x, x
    got = {0: x}
    for s in range(1, n // 2 + 1):
        fwd = shifted(fwd, axis, 1)
        got[-s] = fwd
        if s <= (n - 1) // 2:
            bwd = shifted(bwd, axis, -1)
            got[s] = bwd
    rel = [got[k] if k in got else got[k - n] for k in range(n)]
    rel = jnp.stack(rel + rel)
    me = lax.axis_index(axis)
    return lax.dynamic_slice_in_dim(rel, (n - me) % n, n, 0)


def team_sum(x):
    x = x + shifted(x, "core", 1)
    return x + shifted(x, "xh", 1)


def per_device(loadings, scales, cov):
    n_loads, width = loadings.shape
    groups = scales.shape[1]
    scaled = (
        loadings.astype(jnp.float32).reshape(n_loads, groups, width // groups)
        * scales.astype(jnp.float32)[:, :, None]
    ).reshape(n_loads, width).astype(jnp.bfloat16)
    nz = lax.axis_size("z")
    nt = lax.axis_size("xh") * lax.axis_size("core")
    pairs = []
    for z in range(nz):
        for t in range(nt):
            zh, d = divmod(z, nt)
            pairs.append((z * nt + t, (zh * nt + t) * nt + d))
    moved = lax.ppermute(scaled, ("z", "xh", "core"), pairs)
    s1 = ring_gather(moved, "xl")
    s2 = ring_gather(s1, "z")
    nx = s1.shape[0]
    s2 = s2.reshape(nz // nt, nt, nx, n_loads, width)
    own = jnp.transpose(s2, (3, 2, 0, 1, 4)).reshape(n_loads, nx * nz // nt, nt * width)
    per_y = own.shape[1]
    cov_local = cov[:, :, 0, :]
    ny = lax.axis_size("y")
    me = lax.axis_index("y")

    def term(block, y_from):
        def stop_range(j):
            def run(block, cov_local):
                return lax.dot_general(
                    block,
                    cov_local[:, j * per_y : (j + 1) * per_y, :],
                    (((1, 2), (1, 2)), ((), ())),
                    preferred_element_type=jnp.float32,
                )

            return run

        return lax.switch(y_from % ny, [stop_range(j) for j in range(ny)], block, cov_local)

    part = term(own, me)
    fwd, bwd = own, own
    for s in range(1, ny // 2 + 1):
        fwd = shifted(fwd, "y", 1)
        part = part + term(fwd, me - s)
        if s <= (ny - 1) // 2:
            bwd = shifted(bwd, "y", -1)
            part = part + term(bwd, me + s)
    return team_sum(part)


def solution(mesh):
    sizes = tuple(s for _, s in SUB)
    assert mesh.devices.size == int(np.prod(sizes))
    fine = Mesh(mesh.devices.reshape(sizes), tuple(n for n, _ in SUB))
    placed = (P(None, BLK + TEAM), P(None, BLK + TEAM), P(BLK, None, TEAM, None))
    return jax.shard_map(
        per_device, mesh=fine, in_specs=placed, out_specs=P(None, BLK), check_vma=False
    )
```

```python
import jax
import jax.numpy as jnp
import numpy as np
from jax import lax
from jax.sharding import Mesh
from jax.sharding import PartitionSpec as P

SUB = (("y", 4), ("xl", 2), ("z", 8), ("xh", 2), ("core", 2))
BLK = ("y", "xl", "z")
TEAM = ("xh", "core")


def shifted(x, axis, by):
    n = lax.axis_size(axis)
    return lax.ppermute(x, axis, [(i, (i + by) % n) for i in range(n)])


def ring_gather(x, axis):
    n = lax.axis_size(axis)
    fwd, bwd = x, x
    got = {0: x}
    for s in range(1, n // 2 + 1):
        fwd = shifted(fwd, axis, 1)
        got[-s] = fwd
        if s <= (n - 1) // 2:
            bwd = shifted(bwd, axis, -1)
            got[s] = bwd
    rel = [got[k] if k in got else got[k - n] for k in range(n)]
    rel = jnp.stack(rel + rel)
    me = lax.axis_index(axis)
    return lax.dynamic_slice_in_dim(rel, (n - me) % n, n, 0)


def team_sum(x):
    x = x + shifted(x, "core", 1)
    return x + shifted(x, "xh", 1)


def per_device(loadings, scales, cov):
    n_loads, width = loadings.shape
    groups = scales.shape[1]
    scaled = (
        loadings.astype(jnp.float32).reshape(n_loads, groups, width // groups)
        * scales.astype(jnp.float32)[:, :, None]
    ).reshape(n_loads, width).astype(jnp.bfloat16)
    nz = lax.axis_size("z")
    nt = lax.axis_size("xh") * lax.axis_size("core")
    pairs = []
    for z in range(nz):
        for t in range(nt):
            zh, d = divmod(z, nt)
            pairs.append((z * nt + t, (zh * nt + t) * nt + d))
    moved = lax.ppermute(scaled, ("z", "xh", "core"), pairs)
    s1 = lax.all_gather(moved, "xl")
    s2 = lax.all_gather(s1, "z")
    nx = s1.shape[0]
    s2 = s2.reshape(nz // nt, nt, nx, n_loads, width)
    own = jnp.transpose(s2, (2, 0, 3, 1, 4)).reshape(nx * nz // nt, n_loads, nt * width)
    per_y = own.shape[0]
    cov_local = cov[:, :, 0, :]
    ny = lax.axis_size("y")
    me = lax.axis_index("y")

    def term(block, y_from):
        cov_part = lax.dynamic_slice_in_dim(cov_local, (y_from % ny) * per_y, per_y, 1)
        block, cov_part = lax.optimization_barrier((block, cov_part))
        return lax.dot_general(
            block, cov_part, (((0, 2), (1, 2)), ((), ())), preferred_element_type=jnp.float32
        )

    fwd = shifted(own, "y", 1)
    bwd = shifted(own, "y", -1)
    part = term(own, me)
    part = part + term(fwd, me - 1)
    part = part + term(bwd, me + 1)
    half = n_loads // 2
    far_a = shifted(fwd[:, :half], "y", 1)
    far_b = shifted(bwd[:, half:], "y", -1)
    far = jnp.concatenate([far_a, far_b], axis=1)
    part = part + term(far, me + 2)
    return team_sum(part)


def solution(mesh):
    sizes = tuple(s for _, s in SUB)
    assert mesh.devices.size == int(np.prod(sizes))
    fine = Mesh(mesh.devices.reshape(sizes), tuple(n for n, _ in SUB))
    placed = (P(None, BLK + TEAM), P(None, BLK + TEAM), P(BLK, None, TEAM, None))
    return jax.shard_map(
        per_device, mesh=fine, in_specs=placed, out_specs=P(None, BLK), check_vma=False
    )
```

```python
import jax
import jax.numpy as jnp
import numpy as np
from jax import lax
from jax.sharding import Mesh
from jax.sharding import PartitionSpec as P

SUB = (("y", 4), ("xl", 2), ("z", 8), ("xh", 2), ("core", 2))
BLK = ("y", "xl", "z")
TEAM = ("xh", "core")


def shifted(x, axis, by):
    n = lax.axis_size(axis)
    return lax.ppermute(x, axis, [(i, (i + by) % n) for i in range(n)])


def ring_gather(x, axis):
    n = lax.axis_size(axis)
    fwd, bwd = x, x
    got = {0: x}
    for s in range(1, n // 2 + 1):
        fwd = shifted(fwd, axis, 1)
        got[-s] = fwd
        if s <= (n - 1) // 2:
            bwd = shifted(bwd, axis, -1)
            got[s] = bwd
    rel = [got[k] if k in got else got[k - n] for k in range(n)]
    rel = jnp.stack(rel + rel)
    me = lax.axis_index(axis)
    return lax.dynamic_slice_in_dim(rel, (n - me) % n, n, 0)


def team_sum(x):
    on_chip = x + shifted(x, "core", 1)
    across = shifted(x, "xh", 1) + lax.ppermute(x, ("xh", "core"), [(0, 3), (3, 0), (1, 2), (2, 1)])
    return on_chip + across


def per_device(loadings, scales, cov):
    n_loads, width = loadings.shape
    groups = scales.shape[1]
    scaled = (
        loadings.astype(jnp.float32).reshape(n_loads, groups, width // groups)
        * scales.astype(jnp.float32)[:, :, None]
    ).reshape(n_loads, width).astype(jnp.bfloat16)
    nx = lax.axis_size("xl")
    nz = lax.axis_size("z")
    nt = lax.axis_size("xh") * lax.axis_size("core")
    same, other = [], []
    for x in range(nx):
        for z in range(nz):
            for t in range(nt):
                zh, d = divmod(z, nt)
                src = (x * nz + z) * nt + t
                same.append((src, (x * nz + zh * nt + t) * nt + d))
                other.append((src, (((x + 1) % nx) * nz + zh * nt + t) * nt + d))
    axes = ("xl", "z", "xh", "core")
    mine = lax.ppermute(scaled, axes, same)
    theirs = lax.ppermute(scaled, axes, other)
    first = lax.axis_index("xl") == 0
    s1 = jnp.where(first, jnp.stack([mine, theirs]), jnp.stack([theirs, mine]))
    got = {0: s1}
    for s in range(1, nz // 2):
        got[-s] = shifted(s1, "z", s)
        got[s] = shifted(s1, "z", -s)
    got[-(nz // 2)] = shifted(got[-(nz // 2 - 1)], "z", 1)
    rel = [got[k] if k in got else got[k - nz] for k in range(nz)]
    rel = jnp.stack(rel + rel)
    zme = lax.axis_index("z")
    s2 = lax.dynamic_slice_in_dim(rel, (nz - zme) % nz, nz, 0)
    s2 = s2.reshape(nz // nt, nt, nx, n_loads, width)
    own = jnp.transpose(s2, (2, 0, 3, 1, 4)).reshape(nx * nz // nt, n_loads, nt * width)
    per_y = own.shape[0]
    cov_local = cov[:, :, 0, :]
    ny = lax.axis_size("y")
    me = lax.axis_index("y")

    def term(block, y_from):
        cov_part = lax.dynamic_slice_in_dim(cov_local, (y_from % ny) * per_y, per_y, 1)
        block, cov_part = lax.optimization_barrier((block, cov_part))
        return lax.dot_general(
            block, cov_part, (((0, 2), (1, 2)), ((), ())), preferred_element_type=jnp.float32
        )

    fwd = shifted(own, "y", 1)
    bwd = shifted(own, "y", -1)
    part = term(own, me)
    part = part + term(fwd, me - 1)
    part = part + term(bwd, me + 1)
    half = n_loads // 2
    far_a = shifted(fwd[:, :half], "y", 1)
    far_b = shifted(bwd[:, half:], "y", -1)
    far = jnp.concatenate([far_a, far_b], axis=1)
    part = part + term(far, me + 2)
    return team_sum(part)


def solution(mesh):
    sizes = tuple(s for _, s in SUB)
    assert mesh.devices.size == int(np.prod(sizes))
    fine = Mesh(mesh.devices.reshape(sizes), tuple(n for n, _ in SUB))
    placed = (P(None, BLK + TEAM), P(None, BLK + TEAM), P(BLK, None, TEAM, None))
    return jax.shard_map(
        per_device, mesh=fine, in_specs=placed, out_specs=P(None, BLK), check_vma=False
    )
```

```python
import jax
import jax.numpy as jnp
import numpy as np
from jax import lax
from jax.sharding import Mesh
from jax.sharding import PartitionSpec as P

SUB = (("y", 4), ("xl", 2), ("z", 8), ("xh", 2), ("core", 2))
BLK = ("y", "xl", "z")
TEAM = ("xh", "core")


def shifted(x, axis, by):
    n = lax.axis_size(axis)
    return lax.ppermute(x, axis, [(i, (i + by) % n) for i in range(n)])


def ring_gather(x, axis):
    n = lax.axis_size(axis)
    fwd, bwd = x, x
    got = {0: x}
    for s in range(1, n // 2 + 1):
        fwd = shifted(fwd, axis, 1)
        got[-s] = fwd
        if s <= (n - 1) // 2:
            bwd = shifted(bwd, axis, -1)
            got[s] = bwd
    rel = [got[k] if k in got else got[k - n] for k in range(n)]
    rel = jnp.stack(rel + rel)
    me = lax.axis_index(axis)
    return lax.dynamic_slice_in_dim(rel, (n - me) % n, n, 0)


def team_sum(x):
    x = x + shifted(x, "core", 1)
    return x + shifted(x, "xh", 1)


def per_device(loadings, scales, cov):
    n_loads, width = loadings.shape
    groups = scales.shape[1]
    scaled = (
        loadings.astype(jnp.float32).reshape(n_loads, groups, width // groups)
        * scales.astype(jnp.float32)[:, :, None]
    ).reshape(n_loads, width).astype(jnp.bfloat16)
    nx = lax.axis_size("xl")
    nz = lax.axis_size("z")
    nt = lax.axis_size("xh") * lax.axis_size("core")
    pairs = []
    for z in range(nz):
        for t in range(nt):
            zh, d = divmod(z, nt)
            pairs.append((z * nt + t, (zh * nt + t) * nt + d))
    moved = lax.ppermute(scaled, ("z", "xh", "core"), pairs)
    copies = jnp.broadcast_to(moved[None], (nx * nz,) + moved.shape)
    s2 = lax.all_to_all(copies, ("xl", "z"), 0, 0)
    s2 = s2.reshape(nx, nz // nt, nt, n_loads, width)
    own = jnp.transpose(s2, (0, 1, 3, 2, 4)).reshape(nx * nz // nt, n_loads, nt * width)
    per_y = own.shape[0]
    cov_local = cov[:, :, 0, :]
    ny = lax.axis_size("y")
    me = lax.axis_index("y")

    def term(block, y_from):
        cov_part = lax.dynamic_slice_in_dim(cov_local, (y_from % ny) * per_y, per_y, 1)
        block, cov_part = lax.optimization_barrier((block, cov_part))
        return lax.dot_general(
            block, cov_part, (((0, 2), (1, 2)), ((), ())), preferred_element_type=jnp.float32
        )

    fwd = shifted(own, "y", 1)
    bwd = shifted(own, "y", -1)
    part = term(own, me)
    part = part + term(fwd, me - 1)
    part = part + term(bwd, me + 1)
    half = n_loads // 2
    far_a = shifted(fwd[:, :half], "y", 1)
    far_b = shifted(bwd[:, half:], "y", -1)
    far = jnp.concatenate([far_a, far_b], axis=1)
    part = part + term(far, me + 2)
    return team_sum(part)


def solution(mesh):
    sizes = tuple(s for _, s in SUB)
    assert mesh.devices.size == int(np.prod(sizes))
    fine = Mesh(mesh.devices.reshape(sizes), tuple(n for n, _ in SUB))
    placed = (P(None, BLK + TEAM), P(None, BLK + TEAM), P(BLK, None, TEAM, None))
    return jax.shard_map(
        per_device, mesh=fine, in_specs=placed, out_specs=P(None, BLK), check_vma=False
    )
```

```python
import jax
import jax.numpy as jnp
import numpy as np
from jax import lax
from jax.sharding import Mesh
from jax.sharding import PartitionSpec as P

SUB = (("y", 4), ("xl", 2), ("z", 8), ("xh", 2), ("core", 2))
BLK = ("y", "xl", "z")
TEAM = ("xh", "core")


def shifted(x, axis, by):
    n = lax.axis_size(axis)
    return lax.ppermute(x, axis, [(i, (i + by) % n) for i in range(n)])


def ring_gather(x, axis):
    n = lax.axis_size(axis)
    fwd, bwd = x, x
    got = {0: x}
    for s in range(1, n // 2 + 1):
        fwd = shifted(fwd, axis, 1)
        got[-s] = fwd
        if s <= (n - 1) // 2:
            bwd = shifted(bwd, axis, -1)
            got[s] = bwd
    rel = [got[k] if k in got else got[k - n] for k in range(n)]
    rel = jnp.stack(rel + rel)
    me = lax.axis_index(axis)
    return lax.dynamic_slice_in_dim(rel, (n - me) % n, n, 0)


def team_sum(x):
    x = x + shifted(x, "core", 1)
    return x + shifted(x, "xh", 1)


def per_device(loadings, scales, cov):
    n_loads, width = loadings.shape
    groups = scales.shape[1]
    scaled = (
        loadings.astype(jnp.float32).reshape(n_loads, groups, width // groups)
        * scales.astype(jnp.float32)[:, :, None]
    ).reshape(n_loads, width).astype(jnp.bfloat16)
    nx = lax.axis_size("xl")
    nz = lax.axis_size("z")
    nt = lax.axis_size("xh") * lax.axis_size("core")
    pairs = []
    for z in range(nz):
        for t in range(nt):
            zh, d = divmod(z, nt)
            pairs.append((z * nt + t, (zh * nt + t) * nt + d))
    moved = lax.ppermute(scaled, ("z", "xh", "core"), pairs)
    cov_local = cov[:, :, 0, :]
    ny = lax.axis_size("y")
    me = lax.axis_index("y")
    per_y = nx * nz // nt

    def term(block, y_from):
        cov_part = lax.dynamic_slice_in_dim(cov_local, (y_from % ny) * per_y, per_y, 1)
        block, cov_part = lax.optimization_barrier((block, cov_part))
        return lax.dot_general(
            block, cov_part, (((0, 2), (1, 2)), ((), ())), preferred_element_type=jnp.float32
        )

    def gather_z(piece):
        rows = piece.shape[0]
        copies = jnp.broadcast_to(piece[None], (nx * nz,) + piece.shape)
        s2 = lax.all_to_all(copies, ("xl", "z"), 0, 0)
        s2 = s2.reshape(nx, nz // nt, nt, rows, width)
        return jnp.transpose(s2, (0, 1, 3, 2, 4)).reshape(per_y, rows, nt * width)

    def ring_y(own):
        rows = own.shape[1]
        fwd = shifted(own, "y", 1)
        bwd = shifted(own, "y", -1)
        part = term(own, me)
        part = part + term(fwd, me - 1)
        part = part + term(bwd, me + 1)
        half = rows // 2
        far_a = shifted(fwd[:, :half], "y", 1)
        far_b = shifted(bwd[:, half:], "y", -1)
        far = jnp.concatenate([far_a, far_b], axis=1)
        return team_sum(part + term(far, me + 2))

    split = n_loads // 2
    own_a = gather_z(moved[:split])
    own_a, rest = lax.optimization_barrier((own_a, moved[split:]))
    out_a = ring_y(own_a)
    own_b = gather_z(rest)
    out_b = ring_y(own_b)
    return jnp.concatenate([out_a, out_b], axis=0)


def solution(mesh):
    sizes = tuple(s for _, s in SUB)
    assert mesh.devices.size == int(np.prod(sizes))
    fine = Mesh(mesh.devices.reshape(sizes), tuple(n for n, _ in SUB))
    placed = (P(None, BLK + TEAM), P(None, BLK + TEAM), P(BLK, None, TEAM, None))
    return jax.shard_map(
        per_device, mesh=fine, in_specs=placed, out_specs=P(None, BLK), check_vma=False
    )
```

```python
import jax
import jax.numpy as jnp
import numpy as np
from jax import lax
from jax.sharding import Mesh
from jax.sharding import PartitionSpec as P

SUB = (("y", 4), ("xl", 2), ("z", 8), ("xh", 2), ("core", 2))
BLK = ("y", "xl", "z")
TEAM = ("xh", "core")


def shifted(x, axis, by):
    n = lax.axis_size(axis)
    return lax.ppermute(x, axis, [(i, (i + by) % n) for i in range(n)])


def ring_gather(x, axis):
    n = lax.axis_size(axis)
    fwd, bwd = x, x
    got = {0: x}
    for s in range(1, n // 2 + 1):
        fwd = shifted(fwd, axis, 1)
        got[-s] = fwd
        if s <= (n - 1) // 2:
            bwd = shifted(bwd, axis, -1)
            got[s] = bwd
    rel = [got[k] if k in got else got[k - n] for k in range(n)]
    rel = jnp.stack(rel + rel)
    me = lax.axis_index(axis)
    return lax.dynamic_slice_in_dim(rel, (n - me) % n, n, 0)


def team_sum(x):
    x = x + shifted(x, "core", 1)
    return x + shifted(x, "xh", 1)


def per_device(loadings, scales, cov):
    n_loads, width = loadings.shape
    groups = scales.shape[1]
    scaled = (
        loadings.astype(jnp.float32).reshape(n_loads, groups, width // groups)
        * scales.astype(jnp.float32)[:, :, None]
    ).reshape(n_loads, width).astype(jnp.bfloat16)
    nx = lax.axis_size("xl")
    nz = lax.axis_size("z")
    nt = lax.axis_size("xh") * lax.axis_size("core")
    pairs = []
    for z in range(nz):
        for t in range(nt):
            zh, d = divmod(z, nt)
            pairs.append((z * nt + t, (zh * nt + t) * nt + d))
    moved = lax.ppermute(scaled, ("z", "xh", "core"), pairs)
    ny = lax.axis_size("y")
    copies = jnp.broadcast_to(moved[None], (ny * nx * nz,) + moved.shape)
    s3 = lax.all_to_all(copies, ("y", "xl", "z"), 0, 0)
    s3 = s3.reshape(ny, nx, nz // nt, nt, n_loads, width)
    blocks = jnp.transpose(s3, (0, 1, 2, 4, 3, 5)).reshape(ny, nx * nz // nt, n_loads, nt * width)
    per_y = blocks.shape[1]
    cov_local = cov[:, :, 0, :]
    part = None
    for j in range(ny):
        cov_part = cov_local[:, j * per_y : (j + 1) * per_y, :]
        block, cov_part = lax.optimization_barrier((blocks[j], cov_part))
        term = lax.dot_general(
            block, cov_part, (((0, 2), (1, 2)), ((), ())), preferred_element_type=jnp.float32
        )
        part = term if part is None else part + term
    return team_sum(part)


def solution(mesh):
    sizes = tuple(s for _, s in SUB)
    assert mesh.devices.size == int(np.prod(sizes))
    fine = Mesh(mesh.devices.reshape(sizes), tuple(n for n, _ in SUB))
    placed = (P(None, BLK + TEAM), P(None, BLK + TEAM), P(BLK, None, TEAM, None))
    return jax.shard_map(
        per_device, mesh=fine, in_specs=placed, out_specs=P(None, BLK), check_vma=False
    )
```

```python
import jax
import jax.numpy as jnp
import numpy as np
from jax import lax
from jax.sharding import Mesh
from jax.sharding import PartitionSpec as P

SUB = (("y", 4), ("xl", 2), ("z", 8), ("xh", 2), ("core", 2))
BLK = ("y", "xl", "z")
TEAM = ("xh", "core")


def shifted(x, axis, by):
    n = lax.axis_size(axis)
    return lax.ppermute(x, axis, [(i, (i + by) % n) for i in range(n)])


def ring_gather(x, axis):
    n = lax.axis_size(axis)
    fwd, bwd = x, x
    got = {0: x}
    for s in range(1, n // 2 + 1):
        fwd = shifted(fwd, axis, 1)
        got[-s] = fwd
        if s <= (n - 1) // 2:
            bwd = shifted(bwd, axis, -1)
            got[s] = bwd
    rel = [got[k] if k in got else got[k - n] for k in range(n)]
    rel = jnp.stack(rel + rel)
    me = lax.axis_index(axis)
    return lax.dynamic_slice_in_dim(rel, (n - me) % n, n, 0)


def team_sum(x):
    x = x + shifted(x, "core", 1)
    return x + shifted(x, "xh", 1)


def per_device(loadings, scales, cov):
    n_loads, width = loadings.shape
    groups = scales.shape[1]
    scaled = (
        loadings.astype(jnp.float32).reshape(n_loads, groups, width // groups)
        * scales.astype(jnp.float32)[:, :, None]
    ).reshape(n_loads, width).astype(jnp.bfloat16)
    nx = lax.axis_size("xl")
    nz = lax.axis_size("z")
    nt = lax.axis_size("xh") * lax.axis_size("core")
    pairs = []
    for z in range(nz):
        for t in range(nt):
            zh, d = divmod(z, nt)
            pairs.append((z * nt + t, (zh * nt + t) * nt + d))
    moved = lax.ppermute(scaled, ("z", "xh", "core"), pairs)
    copies = jnp.broadcast_to(moved[None], (nx * nz,) + moved.shape)
    s2 = lax.all_to_all(copies, ("xl", "z"), 0, 0)
    s2 = s2.reshape(nx, nz // nt, nt, n_loads, width)
    own = jnp.transpose(s2, (0, 1, 3, 2, 4)).reshape(nx * nz // nt, n_loads, nt * width)
    per_y = own.shape[0]
    cov_local = cov[:, :, 0, :]
    ny = lax.axis_size("y")
    me = lax.axis_index("y")

    def term(block, y_from):
        cov_part = lax.dynamic_slice_in_dim(cov_local, (y_from % ny) * per_y, per_y, 1)
        block, cov_part = lax.optimization_barrier((block, cov_part))
        return lax.dot_general(
            block, cov_part, (((0, 2), (1, 2)), ((), ())), preferred_element_type=jnp.float32
        )

    half = n_loads // 2
    top, bot = own[:, :half], own[:, half:]
    fwd_top = shifted(top, "y", 1)
    bwd_bot = shifted(bot, "y", -1)
    fwd_bot = shifted(bot, "y", 1)
    bwd_top = shifted(top, "y", -1)
    far_top = shifted(fwd_top, "y", 1)
    far_bot = shifted(bwd_bot, "y", -1)
    part_top = term(top, me) + term(fwd_top, me - 1) + term(bwd_top, me + 1) + term(far_top, me - 2)
    part_bot = term(bot, me) + term(bwd_bot, me + 1) + term(fwd_bot, me - 1) + term(far_bot, me + 2)
    part = jnp.concatenate([part_top, part_bot], axis=0)
    return team_sum(part)


def solution(mesh):
    sizes = tuple(s for _, s in SUB)
    assert mesh.devices.size == int(np.prod(sizes))
    fine = Mesh(mesh.devices.reshape(sizes), tuple(n for n, _ in SUB))
    placed = (P(None, BLK + TEAM), P(None, BLK + TEAM), P(BLK, None, TEAM, None))
    return jax.shard_map(
        per_device, mesh=fine, in_specs=placed, out_specs=P(None, BLK), check_vma=False
    )
```

```python
import jax
import jax.numpy as jnp
import numpy as np
from jax import lax
from jax.sharding import Mesh
from jax.sharding import PartitionSpec as P

SUB = (("y", 4), ("xl", 2), ("z", 8), ("xh", 2), ("core", 2))
BLK = ("y", "xl", "z")
TEAM = ("xh", "core")


def shifted(x, axis, by):
    n = lax.axis_size(axis)
    return lax.ppermute(x, axis, [(i, (i + by) % n) for i in range(n)])


def ring_gather(x, axis):
    n = lax.axis_size(axis)
    fwd, bwd = x, x
    got = {0: x}
    for s in range(1, n // 2 + 1):
        fwd = shifted(fwd, axis, 1)
        got[-s] = fwd
        if s <= (n - 1) // 2:
            bwd = shifted(bwd, axis, -1)
            got[s] = bwd
    rel = [got[k] if k in got else got[k - n] for k in range(n)]
    rel = jnp.stack(rel + rel)
    me = lax.axis_index(axis)
    return lax.dynamic_slice_in_dim(rel, (n - me) % n, n, 0)


def team_sum(x):
    x = x + shifted(x, "core", 1)
    return x + shifted(x, "xh", 1)


def per_device(loadings, scales, cov):
    n_loads, width = loadings.shape
    groups = scales.shape[1]
    scaled = (
        loadings.astype(jnp.float32).reshape(n_loads, groups, width // groups)
        * scales.astype(jnp.float32)[:, :, None]
    ).reshape(n_loads, width).astype(jnp.bfloat16)
    nx = lax.axis_size("xl")
    nz = lax.axis_size("z")
    nt = lax.axis_size("xh") * lax.axis_size("core")
    same, other = [], []
    for x in range(nx):
        for z in range(nz):
            for t in range(nt):
                zh, d = divmod(z, nt)
                src = (x * nz + z) * nt + t
                same.append((src, (x * nz + zh * nt + t) * nt + d))
                other.append((src, (((x + 1) % nx) * nz + zh * nt + t) * nt + d))
    axes = ("xl", "z", "xh", "core")
    mine = lax.ppermute(scaled, axes, same)
    theirs = lax.ppermute(scaled, axes, other)
    first = lax.axis_index("xl") == 0
    s1 = jnp.where(first, jnp.stack([mine, theirs]), jnp.stack([theirs, mine]))
    copies = jnp.broadcast_to(s1[None], (nz,) + s1.shape)
    s2 = lax.all_to_all(copies, "z", 0, 0)
    s2 = jnp.swapaxes(s2, 0, 1)
    s2 = s2.reshape(nx, nz // nt, nt, n_loads, width)
    own = jnp.transpose(s2, (0, 1, 3, 2, 4)).reshape(nx * nz // nt, n_loads, nt * width)
    per_y = own.shape[0]
    cov_local = cov[:, :, 0, :]
    ny = lax.axis_size("y")
    me = lax.axis_index("y")

    def term(block, y_from):
        cov_part = lax.dynamic_slice_in_dim(cov_local, (y_from % ny) * per_y, per_y, 1)
        block, cov_part = lax.optimization_barrier((block, cov_part))
        return lax.dot_general(
            block, cov_part, (((0, 2), (1, 2)), ((), ())), preferred_element_type=jnp.float32
        )

    fwd = shifted(own, "y", 1)
    bwd = shifted(own, "y", -1)
    part = term(own, me)
    part = part + term(fwd, me - 1)
    part = part + term(bwd, me + 1)
    half = n_loads // 2
    far_a = shifted(fwd[:, :half], "y", 1)
    far_b = shifted(bwd[:, half:], "y", -1)
    far = jnp.concatenate([far_a, far_b], axis=1)
    part = part + term(far, me + 2)
    return team_sum(part)


def solution(mesh):
    sizes = tuple(s for _, s in SUB)
    assert mesh.devices.size == int(np.prod(sizes))
    fine = Mesh(mesh.devices.reshape(sizes), tuple(n for n, _ in SUB))
    placed = (P(None, BLK + TEAM), P(None, BLK + TEAM), P(BLK, None, TEAM, None))
    return jax.shard_map(
        per_device, mesh=fine, in_specs=placed, out_specs=P(None, BLK), check_vma=False
    )
```

```python
import jax
import jax.numpy as jnp
import numpy as np
from jax import lax
from jax.sharding import Mesh
from jax.sharding import PartitionSpec as P

SUB = (("y", 4), ("xl", 2), ("z", 8), ("xh", 2), ("core", 2))
BLK = ("y", "xl", "z")
TEAM = ("xh", "core")


def shifted(x, axis, by):
    n = lax.axis_size(axis)
    return lax.ppermute(x, axis, [(i, (i + by) % n) for i in range(n)])


def ring_gather(x, axis):
    n = lax.axis_size(axis)
    fwd, bwd = x, x
    got = {0: x}
    for s in range(1, n // 2 + 1):
        fwd = shifted(fwd, axis, 1)
        got[-s] = fwd
        if s <= (n - 1) // 2:
            bwd = shifted(bwd, axis, -1)
            got[s] = bwd
    rel = [got[k] if k in got else got[k - n] for k in range(n)]
    rel = jnp.stack(rel + rel)
    me = lax.axis_index(axis)
    return lax.dynamic_slice_in_dim(rel, (n - me) % n, n, 0)


def team_sum(x):
    x = x + shifted(x, "core", 1)
    return x + shifted(x, "xh", 1)


def per_device(loadings, scales, cov):
    n_loads, width = loadings.shape
    groups = scales.shape[1]
    scaled = (
        loadings.astype(jnp.float32).reshape(n_loads, groups, width // groups)
        * scales.astype(jnp.float32)[:, :, None]
    ).reshape(n_loads, width).astype(jnp.bfloat16)
    nx = lax.axis_size("xl")
    nz = lax.axis_size("z")
    nt = lax.axis_size("xh") * lax.axis_size("core")
    pairs = []
    for z in range(nz):
        for t in range(nt):
            zh, d = divmod(z, nt)
            pairs.append((z * nt + t, (zh * nt + t) * nt + d))
    moved = lax.ppermute(scaled, ("z", "xh", "core"), pairs)
    copies = jnp.broadcast_to(moved[None], (nx * nz,) + moved.shape)
    s2 = lax.all_to_all(copies, ("xl", "z"), 0, 0)
    per_y = nx * nz // nt
    cov_local = cov[:, :, 0, :]
    ny = lax.axis_size("y")
    me = lax.axis_index("y")
    offsets = (0, -1, 1, 2)
    cov_parts = [
        lax.dynamic_slice_in_dim(cov_local, ((me + k) % ny) * per_y, per_y, 1) for k in offsets
    ]
    s2, cov_parts = lax.optimization_barrier((s2, cov_parts))
    s2 = s2.reshape(nx, nz // nt, nt, n_loads, width)
    own = jnp.transpose(s2, (0, 1, 3, 2, 4)).reshape(per_y, n_loads, nt * width)

    def term(block, k):
        block, cov_part = lax.optimization_barrier((block, cov_parts[offsets.index(k)]))
        return lax.dot_general(
            block, cov_part, (((0, 2), (1, 2)), ((), ())), preferred_element_type=jnp.float32
        )

    fwd = shifted(own, "y", 1)
    bwd = shifted(own, "y", -1)
    part = term(own, 0)
    part = part + term(fwd, -1)
    part = part + term(bwd, 1)
    half = n_loads // 2
    far_a = shifted(fwd[:, :half], "y", 1)
    far_b = shifted(bwd[:, half:], "y", -1)
    far = jnp.concatenate([far_a, far_b], axis=1)
    part = part + term(far, 2)
    return team_sum(part)


def solution(mesh):
    sizes = tuple(s for _, s in SUB)
    assert mesh.devices.size == int(np.prod(sizes))
    fine = Mesh(mesh.devices.reshape(sizes), tuple(n for n, _ in SUB))
    placed = (P(None, BLK + TEAM), P(None, BLK + TEAM), P(BLK, None, TEAM, None))
    return jax.shard_map(
        per_device, mesh=fine, in_specs=placed, out_specs=P(None, BLK), check_vma=False
    )
```

```python
import jax
import jax.numpy as jnp
import numpy as np
from jax import lax
from jax.sharding import Mesh
from jax.sharding import PartitionSpec as P

SUB = (("y", 4), ("xl", 2), ("z", 8), ("xh", 2), ("core", 2))
BLK = ("y", "xl", "z")
TEAM = ("xh", "core")


def shifted(x, axis, by):
    n = lax.axis_size(axis)
    return lax.ppermute(x, axis, [(i, (i + by) % n) for i in range(n)])


def ring_gather(x, axis):
    n = lax.axis_size(axis)
    fwd, bwd = x, x
    got = {0: x}
    for s in range(1, n // 2 + 1):
        fwd = shifted(fwd, axis, 1)
        got[-s] = fwd
        if s <= (n - 1) // 2:
            bwd = shifted(bwd, axis, -1)
            got[s] = bwd
    rel = [got[k] if k in got else got[k - n] for k in range(n)]
    rel = jnp.stack(rel + rel)
    me = lax.axis_index(axis)
    return lax.dynamic_slice_in_dim(rel, (n - me) % n, n, 0)


def team_sum(x):
    x = x + shifted(x, "core", 1)
    return x + shifted(x, "xh", 1)


def per_device(loadings, scales, cov):
    n_loads, width = loadings.shape
    groups = scales.shape[1]
    scaled = (
        loadings.astype(jnp.float32).reshape(n_loads, groups, width // groups)
        * scales.astype(jnp.float32)[:, :, None]
    ).reshape(n_loads, width).astype(jnp.bfloat16)
    nx = lax.axis_size("xl")
    nz = lax.axis_size("z")
    nt = lax.axis_size("xh") * lax.axis_size("core")
    pairs = []
    for z in range(nz):
        for t in range(nt):
            zh, d = divmod(z, nt)
            pairs.append((z * nt + t, (zh * nt + t) * nt + d))
    moved = lax.ppermute(scaled, ("z", "xh", "core"), pairs)
    copies = jnp.broadcast_to(moved[None], (nx * nz,) + moved.shape)
    s2 = lax.all_to_all(copies, ("xl", "z"), 0, 0)
    s2 = s2.reshape(nx, nz // nt, nt, n_loads, width)
    own = jnp.transpose(s2, (0, 1, 3, 2, 4)).reshape(nx * nz // nt, n_loads, nt * width)
    per_y = own.shape[0]
    cov_local = cov[:, :, 0, :]
    ny = lax.axis_size("y")
    me = lax.axis_index("y")

    def term(block, y_from):
        cov_part = lax.dynamic_slice_in_dim(cov_local, (y_from % ny) * per_y, per_y, 1)
        block, cov_part = lax.optimization_barrier((block, cov_part))
        return lax.dot_general(
            block, cov_part, (((0, 2), (1, 2)), ((), ())), preferred_element_type=jnp.float32
        )

    fwd = shifted(own, "y", 1)
    bwd = shifted(own, "y", -1)
    part = term(own, me)
    part = part + term(fwd, me - 1)
    part = part + term(bwd, me + 1)
    half = n_loads // 2
    far_a = shifted(fwd[:, :half], "y", 1)
    far_b = shifted(bwd[:, half:], "y", -1)
    far = jnp.concatenate([far_a, far_b], axis=1)
    return team_sum(part) + team_sum(term(far, me + 2))


def solution(mesh):
    sizes = tuple(s for _, s in SUB)
    assert mesh.devices.size == int(np.prod(sizes))
    fine = Mesh(mesh.devices.reshape(sizes), tuple(n for n, _ in SUB))
    placed = (P(None, BLK + TEAM), P(None, BLK + TEAM), P(BLK, None, TEAM, None))
    return jax.shard_map(
        per_device, mesh=fine, in_specs=placed, out_specs=P(None, BLK), check_vma=False
    )
```

```python
import jax
import jax.numpy as jnp
import numpy as np
from jax import lax
from jax.sharding import Mesh
from jax.sharding import PartitionSpec as P

SUB = (("y", 4), ("xl", 2), ("z", 8), ("xh", 2), ("core", 2))
BLK = ("y", "xl", "z")
TEAM = ("xh", "core")


def shifted(x, axis, by):
    n = lax.axis_size(axis)
    return lax.ppermute(x, axis, [(i, (i + by) % n) for i in range(n)])


def ring_gather(x, axis):
    n = lax.axis_size(axis)
    fwd, bwd = x, x
    got = {0: x}
    for s in range(1, n // 2 + 1):
        fwd = shifted(fwd, axis, 1)
        got[-s] = fwd
        if s <= (n - 1) // 2:
            bwd = shifted(bwd, axis, -1)
            got[s] = bwd
    rel = [got[k] if k in got else got[k - n] for k in range(n)]
    rel = jnp.stack(rel + rel)
    me = lax.axis_index(axis)
    return lax.dynamic_slice_in_dim(rel, (n - me) % n, n, 0)


def team_sum(x):
    x = x + shifted(x, "core", 1)
    return x + shifted(x, "xh", 1)


def per_device(loadings, scales, cov):
    n_loads, width = loadings.shape
    groups = scales.shape[1]
    scaled = (
        loadings.astype(jnp.float32).reshape(n_loads, groups, width // groups)
        * scales.astype(jnp.float32)[:, :, None]
    ).reshape(n_loads, width).astype(jnp.bfloat16)
    nx = lax.axis_size("xl")
    nz = lax.axis_size("z")
    nt = lax.axis_size("xh") * lax.axis_size("core")
    pairs = []
    for z in range(nz):
        for t in range(nt):
            zh, d = divmod(z, nt)
            pairs.append((z * nt + t, (zh * nt + t) * nt + d))
    moved = lax.ppermute(scaled, ("z", "xh", "core"), pairs)
    copies = jnp.broadcast_to(moved[None], (nx * nz,) + moved.shape)
    s2 = lax.all_to_all(copies, ("xl", "z"), 0, 0)
    s2 = s2.reshape(nx, nz // nt, nt, n_loads, width)
    own = jnp.transpose(s2, (0, 1, 3, 2, 4)).reshape(nx * nz // nt, n_loads, nt * width)
    per_y = own.shape[0]
    cov_local = cov[:, :, 0, :]
    ny = lax.axis_size("y")
    me = lax.axis_index("y")

    def term(block, y_from):
        cov_part = lax.dynamic_slice_in_dim(cov_local, (y_from % ny) * per_y, per_y, 1)
        block, cov_part = lax.optimization_barrier((block, cov_part))
        return lax.dot_general(
            block, cov_part, (((0, 2), (1, 2)), ((), ())), preferred_element_type=jnp.float32
        )

    fwd = shifted(own, "y", 1)
    bwd = shifted(own, "y", -1)
    part = term(own, me)
    part = part + term(fwd, me - 1)
    part = part + term(bwd, me + 1)
    half = n_loads // 2
    far_a = shifted(fwd[:, :half], "y", 1)
    far_b = shifted(bwd[:, half:], "y", -1)
    far = jnp.concatenate([far_a, far_b], axis=1)
    early, far = lax.optimization_barrier((team_sum(part), far))
    return early + team_sum(term(far, me + 2))


def solution(mesh):
    sizes = tuple(s for _, s in SUB)
    assert mesh.devices.size == int(np.prod(sizes))
    fine = Mesh(mesh.devices.reshape(sizes), tuple(n for n, _ in SUB))
    placed = (P(None, BLK + TEAM), P(None, BLK + TEAM), P(BLK, None, TEAM, None))
    return jax.shard_map(
        per_device, mesh=fine, in_specs=placed, out_specs=P(None, BLK), check_vma=False
    )
```

```python
import jax
import jax.numpy as jnp
import numpy as np
from jax import lax
from jax.sharding import Mesh
from jax.sharding import PartitionSpec as P

SUB = (("y", 4), ("xl", 2), ("z", 8), ("xh", 2), ("core", 2))
BLK = ("y", "xl", "z")
TEAM = ("xh", "core")


def shifted(x, axis, by):
    n = lax.axis_size(axis)
    return lax.ppermute(x, axis, [(i, (i + by) % n) for i in range(n)])


def ring_gather(x, axis):
    n = lax.axis_size(axis)
    fwd, bwd = x, x
    got = {0: x}
    for s in range(1, n // 2 + 1):
        fwd = shifted(fwd, axis, 1)
        got[-s] = fwd
        if s <= (n - 1) // 2:
            bwd = shifted(bwd, axis, -1)
            got[s] = bwd
    rel = [got[k] if k in got else got[k - n] for k in range(n)]
    rel = jnp.stack(rel + rel)
    me = lax.axis_index(axis)
    return lax.dynamic_slice_in_dim(rel, (n - me) % n, n, 0)


def team_sum(x):
    x = x + shifted(x, "core", 1)
    return x + shifted(x, "xh", 1)


def per_device(loadings, scales, cov):
    n_loads, width = loadings.shape
    groups = scales.shape[1]
    scaled = (
        loadings.astype(jnp.float32).reshape(n_loads, groups, width // groups)
        * scales.astype(jnp.float32)[:, :, None]
    ).reshape(n_loads, width).astype(jnp.bfloat16)
    nx = lax.axis_size("xl")
    nz = lax.axis_size("z")
    nt = lax.axis_size("xh") * lax.axis_size("core")
    pairs = []
    for z in range(nz):
        for t in range(nt):
            zh, d = divmod(z, nt)
            pairs.append((z * nt + t, (zh * nt + t) * nt + d))
    moved = lax.ppermute(scaled, ("z", "xh", "core"), pairs)
    copies = jnp.broadcast_to(moved[None], (nx * nz,) + moved.shape)
    s2 = lax.all_to_all(copies, ("xl", "z"), 0, 0)
    s2 = s2.reshape(nx, nz // nt, nt, n_loads, width)
    own = jnp.transpose(s2, (0, 1, 3, 2, 4)).reshape(nx * nz // nt, n_loads, nt * width)
    per_y = own.shape[0]
    cov_local = cov[:, :, 0, :]
    ny = lax.axis_size("y")
    me = lax.axis_index("y")

    def term(block, y_from):
        cov_part = lax.dynamic_slice_in_dim(cov_local, (y_from % ny) * per_y, per_y, 1)
        block, cov_part = lax.optimization_barrier((block, cov_part))
        return lax.dot_general(
            block, cov_part, (((0, 2), (1, 2)), ((), ())), preferred_element_type=jnp.float32
        )

    fwd = shifted(own, "y", 1)
    bwd = shifted(own, "y", -1)
    part = term(own, me)
    part = part + term(fwd, me - 1)
    part = part + term(bwd, me + 1)
    half = n_loads // 2
    far_a = shifted(fwd[:, :half], "y", 1)
    far_b = shifted(bwd[:, half:], "y", -1)
    far = jnp.concatenate([far_a, far_b], axis=1)
    pair = part + shifted(part, "core", 1)
    far_term = term(far, me + 2)
    pair = pair + (far_term + shifted(far_term, "core", 1))
    return pair + shifted(pair, "xh", 1)


def solution(mesh):
    sizes = tuple(s for _, s in SUB)
    assert mesh.devices.size == int(np.prod(sizes))
    fine = Mesh(mesh.devices.reshape(sizes), tuple(n for n, _ in SUB))
    placed = (P(None, BLK + TEAM), P(None, BLK + TEAM), P(BLK, None, TEAM, None))
    return jax.shard_map(
        per_device, mesh=fine, in_specs=placed, out_specs=P(None, BLK), check_vma=False
    )
```

```python
import jax
import jax.numpy as jnp
import numpy as np
from jax import lax
from jax.sharding import Mesh
from jax.sharding import PartitionSpec as P

SUB = (("y", 4), ("xl", 2), ("z", 8), ("xh", 2), ("core", 2))
BLK = ("y", "xl", "z")
TEAM = ("xh", "core")


def shifted(x, axis, by):
    n = lax.axis_size(axis)
    return lax.ppermute(x, axis, [(i, (i + by) % n) for i in range(n)])


def ring_gather(x, axis):
    n = lax.axis_size(axis)
    fwd, bwd = x, x
    got = {0: x}
    for s in range(1, n // 2 + 1):
        fwd = shifted(fwd, axis, 1)
        got[-s] = fwd
        if s <= (n - 1) // 2:
            bwd = shifted(bwd, axis, -1)
            got[s] = bwd
    rel = [got[k] if k in got else got[k - n] for k in range(n)]
    rel = jnp.stack(rel + rel)
    me = lax.axis_index(axis)
    return lax.dynamic_slice_in_dim(rel, (n - me) % n, n, 0)


def team_sum(x):
    x = x + shifted(x, "core", 1)
    return x + shifted(x, "xh", 1)


def per_device(loadings, scales, cov):
    n_loads, width = loadings.shape
    groups = scales.shape[1]
    scaled = (
        loadings.astype(jnp.float32).reshape(n_loads, groups, width // groups)
        * scales.astype(jnp.float32)[:, :, None]
    ).reshape(n_loads, width).astype(jnp.bfloat16)
    nx = lax.axis_size("xl")
    nz = lax.axis_size("z")
    nt = lax.axis_size("xh") * lax.axis_size("core")
    pairs = []
    for z in range(nz):
        for t in range(nt):
            zh, d = divmod(z, nt)
            pairs.append((z * nt + t, (zh * nt + t) * nt + d))
    moved = lax.ppermute(scaled, ("z", "xh", "core"), pairs)
    copies = jnp.broadcast_to(moved[None], (nx * nz,) + moved.shape)
    s2 = lax.all_to_all(copies, ("xl", "z"), 0, 0)
    s2 = s2.reshape(nx, nz // nt, nt, n_loads, width)
    own = jnp.transpose(s2, (0, 1, 3, 2, 4)).reshape(nx * nz // nt, n_loads, nt * width)
    per_y = own.shape[0]
    cov_local = cov[:, :, 0, :]
    ny = lax.axis_size("y")
    me = lax.axis_index("y")

    def term(block, y_from):
        cov_part = lax.dynamic_slice_in_dim(cov_local, (y_from % ny) * per_y, per_y, 1)
        block, cov_part = lax.optimization_barrier((block, cov_part))
        return lax.dot_general(
            block, cov_part, (((0, 2), (1, 2)), ((), ())), preferred_element_type=jnp.float32
        )

    fwd = shifted(own, "y", 1)
    bwd = shifted(own, "y", -1)
    part = term(own, me)
    part = part + term(fwd, me - 1)
    part = part + term(bwd, me + 1)
    half = n_loads // 2
    far_a = shifted(fwd[:, :half], "y", 1)
    far_b = shifted(bwd[:, half:], "y", -1)
    far = jnp.concatenate([far_a, far_b], axis=1)
    pair = part + shifted(part, "core", 1)
    far_term = term(far, me + 2)
    f_core = shifted(far_term, "core", 1)
    f_diag = lax.ppermute(far_term, ("xh", "core"), [(0, 3), (3, 0), (1, 2), (2, 1)])
    other = shifted(jnp.stack([pair, far_term]), "xh", 1)
    mine = pair + (far_term + f_core)
    theirs = other[0] + (other[1] + f_diag)
    return mine + theirs


def solution(mesh):
    sizes = tuple(s for _, s in SUB)
    assert mesh.devices.size == int(np.prod(sizes))
    fine = Mesh(mesh.devices.reshape(sizes), tuple(n for n, _ in SUB))
    placed = (P(None, BLK + TEAM), P(None, BLK + TEAM), P(BLK, None, TEAM, None))
    return jax.shard_map(
        per_device, mesh=fine, in_specs=placed, out_specs=P(None, BLK), check_vma=False
    )
```

```python
import jax
import jax.numpy as jnp
import numpy as np
from jax import lax
from jax.sharding import Mesh
from jax.sharding import PartitionSpec as P

SUB = (("y", 4), ("xl", 2), ("z", 8), ("xh", 2), ("core", 2))
BLK = ("y", "xl", "z")
TEAM = ("xh", "core")


def shifted(x, axis, by):
    n = lax.axis_size(axis)
    return lax.ppermute(x, axis, [(i, (i + by) % n) for i in range(n)])


def ring_gather(x, axis):
    n = lax.axis_size(axis)
    fwd, bwd = x, x
    got = {0: x}
    for s in range(1, n // 2 + 1):
        fwd = shifted(fwd, axis, 1)
        got[-s] = fwd
        if s <= (n - 1) // 2:
            bwd = shifted(bwd, axis, -1)
            got[s] = bwd
    rel = [got[k] if k in got else got[k - n] for k in range(n)]
    rel = jnp.stack(rel + rel)
    me = lax.axis_index(axis)
    return lax.dynamic_slice_in_dim(rel, (n - me) % n, n, 0)


def team_sum(x):
    x = x + shifted(x, "core", 1)
    return x + shifted(x, "xh", 1)


def per_device(loadings, scales, cov):
    n_loads, width = loadings.shape
    groups = scales.shape[1]
    scaled = (
        loadings.astype(jnp.float32).reshape(n_loads, groups, width // groups)
        * scales.astype(jnp.float32)[:, :, None]
    ).reshape(n_loads, width).astype(jnp.bfloat16)
    nx = lax.axis_size("xl")
    nz = lax.axis_size("z")
    nt = lax.axis_size("xh") * lax.axis_size("core")
    pairs = []
    for z in range(nz):
        for t in range(nt):
            zh, d = divmod(z, nt)
            pairs.append((z * nt + t, (zh * nt + t) * nt + d))
    moved = lax.ppermute(scaled, ("z", "xh", "core"), pairs)
    copies = jnp.broadcast_to(moved[None], (nx * nz,) + moved.shape)
    s2 = lax.all_to_all(copies, ("xl", "z"), 0, 0)
    own = s2
    per_y = nx * nz // nt
    cov_local = cov[:, :, 0, :]
    ny = lax.axis_size("y")
    me = lax.axis_index("y")

    def term(block, y_from):
        cov_part = lax.dynamic_slice_in_dim(cov_local, (y_from % ny) * per_y, per_y, 1)
        cov_part = cov_part.reshape(cov_part.shape[0], nx, nz // nt, nt, width)
        block = block.reshape(nx, nz // nt, nt, block.shape[1], width)
        block, cov_part = lax.optimization_barrier((block, cov_part))
        return lax.dot_general(
            block, cov_part, (((0, 1, 2, 4), (1, 2, 3, 4)), ((), ())), preferred_element_type=jnp.float32
        )

    fwd = shifted(own, "y", 1)
    bwd = shifted(own, "y", -1)
    part = term(own, me)
    part = part + term(fwd, me - 1)
    part = part + term(bwd, me + 1)
    half = n_loads // 2
    far_a = shifted(fwd[:, :half], "y", 1)
    far_b = shifted(bwd[:, half:], "y", -1)
    far = jnp.concatenate([far_a, far_b], axis=1)
    pair = part + shifted(part, "core", 1)
    far_term = term(far, me + 2)
    pair = pair + (far_term + shifted(far_term, "core", 1))
    return pair + shifted(pair, "xh", 1)


def solution(mesh):
    sizes = tuple(s for _, s in SUB)
    assert mesh.devices.size == int(np.prod(sizes))
    fine = Mesh(mesh.devices.reshape(sizes), tuple(n for n, _ in SUB))
    placed = (P(None, BLK + TEAM), P(None, BLK + TEAM), P(BLK, None, TEAM, None))
    return jax.shard_map(
        per_device, mesh=fine, in_specs=placed, out_specs=P(None, BLK), check_vma=False
    )
```
